256 devices in a mesh: gx: 32 (over y, z), gy: 4 (over x_hi, core), col: 2 (over x_lo).
Axes of the slice: x: 4 (x_hi: 2, x_lo: 2; x = x_hi * 2 + x_lo), y: 4, z: 8, core: 2. Of those that a mesh axis runs over, the one named last changes fastest.
Arguments:
- inputs: bfloat16 [64, 2, 512, 512], P('col', None, 'gx', 'gy'), may hold values from -6 to 6
- cotangent: bfloat16 [64, 2, 512, 512], P('col', None, 'gx', 'gy'), may hold values from -6 to 6
- first_weight: bfloat16 [64, 64, 3, 3, 3], replicated, may hold values from -0.15625 to 0.15625
- second_weight: bfloat16 [64, 64, 3, 3, 3], replicated, may hold values from -0.15625 to 0.15625
Outputs:
- features: bfloat16 [64, 2, 512, 512], P('col', None, 'gx', 'gy')
- input_grad: bfloat16 [64, 2, 512, 512], P('col', None, 'gx', 'gy')
The draws below stay inside these ranges and needn't reach their ends.
All inputs are finite; a program needn't handle non-finite values.
Results may differ from the reference program's by a relative error of at most 0.015.
Values may be sent and summed in bfloat16 or wider, within the bound.
No kernel may reach another device: no remote copies, remote signals or barrier semaphores. Data moves between devices by JAX's collectives and lax.ppermute only.
A program may use at most 64 MiB of HBM per device.

```python
import jax
import jax.numpy as jnp
from jax import lax

C = 64
ZP = 2
NX = 512
NY = 512


def levels(key, dims, pieces, smallest, top_value):
    gain, own = 1.0, jax.random.fold_in(key, 6)
    for dim, parts in pieces:
        heights = jnp.exp(jax.random.uniform(jax.random.fold_in(own, dim), (parts,), jnp.float32, smallest / len(pieces), top_value / len(pieces)))
        gain = gain * jnp.repeat(heights, dims[dim] // parts).reshape([-1 if axis == dim else 1 for axis in range(len(dims))])
    return gain


def scatter_about(rng, shape, scale, bound, shards=(), kind=jnp.bfloat16):
    factor_of = levels(rng, shape, shards, -0.22, 0.18) if shards else 1.0
    values = jax.random.normal(rng, shape, jnp.float32) * scale * factor_of
    return jnp.minimum(jnp.maximum(values, -bound), bound).astype(kind)


def setup_inputs(seed: int = 0) -> dict:
    key_list = jax.random.split(jax.random.key(seed), 5)
    inputs = scatter_about(key_list[0], (C, ZP, NX, NY), 1.0, 6.0, ((0, 2), (2, 32), (3, 4)))
    cotangent = scatter_about(key_list[1], (C, ZP, NX, NY), 1.0, 6.0, ((0, 2), (2, 32), (3, 4)))
    first_weight = scatter_about(key_list[2], (C, C, 3, 3, 3), (27 * C) ** -0.5, 0.15625)
    second_weight = scatter_about(key_list[3], (C, C, 3, 3, 3), (27 * C) ** -0.5, 0.15625)
    return {"inputs": inputs, "cotangent": cotangent, "first_weight": first_weight, "second_weight": second_weight}


def convolve(field, weight):
    padded = jnp.pad(field, ((0, 0), (1, 1), (0, 0), (0, 0)))
    padded = jnp.concatenate([padded[:, :, -1:], padded, padded[:, :, :1]], axis=2)
    padded = jnp.concatenate([padded[:, :, :, -1:], padded, padded[:, :, :, :1]], axis=3)
    result = lax.conv_general_dilated(padded[None], weight, (1, 1, 1), "VALID",
                                      dimension_numbers=("NCDHW", "OIDHW", "NCDHW"),
                                      precision=lax.Precision.HIGHEST)
    return result[0]


def flipped(weight):
    return jnp.transpose(jnp.flip(weight, (2, 3, 4)), (1, 0, 2, 3, 4))


def reference(inputs, cotangent, first_weight, second_weight):
    first = first_weight.astype(jnp.float32)
    second = second_weight.astype(jnp.float32)
    pre = convolve(inputs.astype(jnp.float32), first)
    act = jax.nn.silu(pre).astype(jnp.bfloat16)
    features = convolve(act.astype(jnp.float32), second).astype(jnp.bfloat16)
    back = convolve(cotangent.astype(jnp.float32), flipped(second))
    sigma = jax.nn.sigmoid(pre)
    act_grad = (back * (sigma * (1.0 + pre * (1.0 - sigma)))).astype(jnp.bfloat16)
    input_grad = convolve(act_grad.astype(jnp.float32), flipped(first)).astype(jnp.bfloat16)
    return features, input_grad
```

```python
import jax
import jax.numpy as jnp
from jax import lax
from jax.sharding import PartitionSpec as P


def _span(d, n):
    if d < 0:
        return n - 1, n
    if d > 0:
        return 0, 1
    return 0, n


def padded_block(block):
    nx, ny = lax.axis_size("gx"), lax.axis_size("gy")
    X, Y = block.shape[2], block.shape[3]
    pieces = {}
    for dx in (-1, 0, 1):
        for dy in (-1, 0, 1):
            if dx == 0 and dy == 0:
                pieces[(dx, dy)] = block
                continue
            x0, x1 = _span(dx, X)
            y0, y1 = _span(dy, Y)
            part = block[:, :, x0:x1, y0:y1]
            pairs = []
            for i in range(nx):
                for j in range(ny):
                    src = i * ny + j
                    dst = ((i - dx) % nx) * ny + (j - dy) % ny
                    pairs.append((src, dst))
            pieces[(dx, dy)] = lax.ppermute(part, ("gx", "gy"), pairs)
    rows = []
    for dx in (-1, 0, 1):
        rows.append(jnp.concatenate([pieces[(dx, -1)], pieces[(dx, 0)], pieces[(dx, 1)]], axis=3))
    return jnp.concatenate(rows, axis=2)


def local_conv(piece, weight):
    result = lax.conv_general_dilated(
        piece[None],
        weight,
        (1, 1, 1),
        "VALID",
        dimension_numbers=("NCDHW", "OIDHW", "NCDHW"),
        preferred_element_type=jnp.float32,
    )
    return result[0]


def flipped(weight):
    return jnp.transpose(jnp.flip(weight, (2, 3, 4)), (1, 0, 2, 3, 4))


def ordered(weight, owned):
    col = lax.axis_index("col")
    rows = lax.dynamic_slice_in_dim(weight, col * owned, owned, 0)
    mine = lax.dynamic_slice_in_dim(rows, col * owned, owned, 1)
    other = lax.dynamic_slice_in_dim(rows, (1 - col) * owned, owned, 1)
    return jnp.concatenate([mine, other], axis=1)


def convolve_pair(a, b, wa, wb):
    owned = a.shape[0]
    both = jnp.concatenate([a, b], axis=0)
    padded = padded_block(both)
    partner = lax.ppermute(padded, "col", [(0, 1), (1, 0)])
    full = jnp.concatenate([padded, partner], axis=0)
    full = jnp.pad(full, ((0, 0), (1, 1), (0, 0), (0, 0)))
    fa = jnp.concatenate([full[:owned], full[2 * owned:3 * owned]], axis=0)
    fb = jnp.concatenate([full[owned:2 * owned], full[3 * owned:]], axis=0)
    return local_conv(fa, ordered(wa, owned)), local_conv(fb, ordered(wb, owned))


def on_device(inputs, cotangent, first_weight, second_weight):
    pre, back = convolve_pair(inputs, cotangent, first_weight, flipped(second_weight))
    act = jax.nn.silu(pre).astype(jnp.bfloat16)
    sigma = jax.nn.sigmoid(pre)
    act_grad = (back * (sigma * (1.0 + pre * (1.0 - sigma)))).astype(jnp.bfloat16)
    features, input_grad = convolve_pair(act, act_grad, second_weight, flipped(first_weight))
    return (features.astype(jnp.bfloat16), input_grad.astype(jnp.bfloat16))


def solution(mesh):
    placed = (P("col", None, "gx", "gy"), P("col", None, "gx", "gy"), P(), P())
    return jax.shard_map(
        on_device,
        mesh=mesh,
        in_specs=placed,
        out_specs=(P("col", None, "gx", "gy"), P("col", None, "gx", "gy")),
        check_vma=False,
    )
```

```python
import jax
import jax.numpy as jnp
from jax import lax
from jax.sharding import PartitionSpec as P


def _span(d, n):
    if d < 0:
        return n - 1, n
    if d > 0:
        return 0, 1
    return 0, n


OFFSETS = [(dx, dy) for dx in (-1, 0, 1) for dy in (-1, 0, 1) if (dx, dy) != (0, 0)]


def halo_pieces(block):
    nx, ny = lax.axis_size("gx"), lax.axis_size("gy")
    X, Y = block.shape[2], block.shape[3]
    pieces = []
    for dx, dy in OFFSETS:
        x0, x1 = _span(dx, X)
        y0, y1 = _span(dy, Y)
        part = block[:, :, x0:x1, y0:y1].reshape(-1)
        pairs = []
        for i in range(nx):
            for j in range(ny):
                pairs.append((i * ny + j, ((i - dx) % nx) * ny + (j - dy) % ny))
        pieces.append(lax.ppermute(part, ("gx", "gy"), pairs))
    return pieces


def assemble(block, pieces):
    C, Z, X, Y = block.shape
    got = {(0, 0): block}
    for (dx, dy), flat in zip(OFFSETS, pieces):
        x0, x1 = _span(dx, X)
        y0, y1 = _span(dy, Y)
        got[(dx, dy)] = flat.reshape(C, Z, x1 - x0, y1 - y0)
    rows = [jnp.concatenate([got[(dx, -1)], got[(dx, 0)], got[(dx, 1)]], axis=3) for dx in (-1, 0, 1)]
    return jnp.concatenate(rows, axis=2)


def padded_pair(block):
    C, Z, X, Y = block.shape
    pieces = halo_pieces(block)
    lanes = Y
    halo = jnp.concatenate(pieces)
    extra = (-halo.shape[0]) % lanes
    halo = jnp.pad(halo, (0, extra))
    message = jnp.concatenate([block.reshape(-1, lanes), halo.reshape(-1, lanes)], axis=0)
    got = lax.ppermute(message, "col", [(0, 1), (1, 0)])
    other = got[: C * Z * X].reshape(C, Z, X, Y)
    flat = got[C * Z * X:].reshape(-1)
    sizes = [p.shape[0] for p in pieces]
    theirs = []
    at = 0
    for n in sizes:
        theirs.append(flat[at:at + n])
        at += n
    return assemble(block, pieces), assemble(other, theirs)


def local_conv(piece, weight):
    result = lax.conv_general_dilated(
        piece[None],
        weight,
        (1, 1, 1),
        "VALID",
        dimension_numbers=("NCDHW", "OIDHW", "NCDHW"),
        preferred_element_type=jnp.float32,
    )
    return result[0]


def flipped(weight):
    return jnp.transpose(jnp.flip(weight, (2, 3, 4)), (1, 0, 2, 3, 4))


def ordered(weight, owned):
    col = lax.axis_index("col")
    rows = lax.dynamic_slice_in_dim(weight, col * owned, owned, 0)
    mine = lax.dynamic_slice_in_dim(rows, col * owned, owned, 1)
    other = lax.dynamic_slice_in_dim(rows, (1 - col) * owned, owned, 1)
    return jnp.concatenate([mine, other], axis=1)


def convolve_pair(a, b, wa, wb):
    owned = a.shape[0]
    both = jnp.concatenate([a, b], axis=0)
    padded, partner = padded_pair(both)
    full = jnp.concatenate([padded, partner], axis=0)
    full = jnp.pad(full, ((0, 0), (1, 1), (0, 0), (0, 0)))
    fa = jnp.concatenate([full[:owned], full[2 * owned:3 * owned]], axis=0)
    fb = jnp.concatenate([full[owned:2 * owned], full[3 * owned:]], axis=0)
    return local_conv(fa, ordered(wa, owned)), local_conv(fb, ordered(wb, owned))


def on_device(inputs, cotangent, first_weight, second_weight):
    pre, back = convolve_pair(inputs, cotangent, first_weight, flipped(second_weight))
    act = jax.nn.silu(pre).astype(jnp.bfloat16)
    sigma = jax.nn.sigmoid(pre)
    act_grad = (back * (sigma * (1.0 + pre * (1.0 - sigma)))).astype(jnp.bfloat16)
    features, input_grad = convolve_pair(act, act_grad, second_weight, flipped(first_weight))
    return (features.astype(jnp.bfloat16), input_grad.astype(jnp.bfloat16))


def solution(mesh):
    placed = (P("col", None, "gx", "gy"), P("col", None, "gx", "gy"), P(), P())
    return jax.shard_map(
        on_device,
        mesh=mesh,
        in_specs=placed,
        out_specs=(P("col", None, "gx", "gy"), P("col", None, "gx", "gy")),
        check_vma=False,
    )
```

```python
import jax
import jax.numpy as jnp
from jax import lax
from jax.sharding import PartitionSpec as P


def _span(d, n):
    if d < 0:
        return n - 1, n
    if d > 0:
        return 0, 1
    return 0, n


OFFSETS = [(dx, dy) for dx in (-1, 0, 1) for dy in (-1, 0, 1) if (dx, dy) != (0, 0)]


def halo_pieces(block):
    nx, ny = lax.axis_size("gx"), lax.axis_size("gy")
    X, Y = block.shape[1], block.shape[2]
    pieces = []
    for dx, dy in OFFSETS:
        x0, x1 = _span(dx, X)
        y0, y1 = _span(dy, Y)
        part = block[:, x0:x1, y0:y1, :].reshape(-1)
        pairs = []
        for i in range(nx):
            for j in range(ny):
                pairs.append((i * ny + j, ((i - dx) % nx) * ny + (j - dy) % ny))
        pieces.append(lax.ppermute(part, ("gx", "gy"), pairs))
    return pieces


def assemble(block, pieces):
    Z, X, Y, C = block.shape
    got = {(0, 0): block}
    for (dx, dy), flat in zip(OFFSETS, pieces):
        x0, x1 = _span(dx, X)
        y0, y1 = _span(dy, Y)
        got[(dx, dy)] = flat.reshape(Z, x1 - x0, y1 - y0, C)
    rows = [jnp.concatenate([got[(dx, -1)], got[(dx, 0)], got[(dx, 1)]], axis=2) for dx in (-1, 0, 1)]
    return jnp.concatenate(rows, axis=1)


def padded_pair(block):
    lanes = 128
    pieces = halo_pieces(block)
    halo = jnp.concatenate(pieces)
    halo = jnp.pad(halo, (0, (-halo.shape[0]) % lanes))
    body = block.reshape(-1)
    message = jnp.concatenate([body, halo]).reshape(-1, lanes)
    got = lax.ppermute(message, "col", [(0, 1), (1, 0)]).reshape(-1)
    other = got[: body.shape[0]].reshape(block.shape)
    theirs = []
    at = body.shape[0]
    for p in pieces:
        theirs.append(got[at:at + p.shape[0]])
        at += p.shape[0]
    return assemble(block, pieces), assemble(other, theirs)


def local_conv(piece, weight):
    result = lax.conv_general_dilated(
        piece[None],
        weight,
        (1, 1, 1),
        ((1, 1), (0, 0), (0, 0)),
        dimension_numbers=("NDHWC", "DHWIO", "NDHWC"),
        preferred_element_type=jnp.float32,
    )
    return result[0]


def flipped(weight):
    return jnp.transpose(jnp.flip(weight, (2, 3, 4)), (1, 0, 2, 3, 4))


def ordered(weight, owned):
    col = lax.axis_index("col")
    rows = lax.dynamic_slice_in_dim(weight, col * owned, owned, 0)
    mine = lax.dynamic_slice_in_dim(rows, col * owned, owned, 1)
    other = lax.dynamic_slice_in_dim(rows, (1 - col) * owned, owned, 1)
    return jnp.transpose(jnp.concatenate([mine, other], axis=1), (2, 3, 4, 1, 0))


def convolve_pair(both, owned, wa, wb):
    padded, partner = padded_pair(both)
    fa = jnp.concatenate([padded[..., :owned], partner[..., :owned]], axis=-1)
    fb = jnp.concatenate([padded[..., owned:], partner[..., owned:]], axis=-1)
    return local_conv(fa, ordered(wa, owned)), local_conv(fb, ordered(wb, owned))


def on_device(inputs, cotangent, first_weight, second_weight):
    owned = inputs.shape[0]
    both = jnp.transpose(jnp.concatenate([inputs, cotangent], axis=0), (1, 2, 3, 0))
    pre, back = convolve_pair(both, owned, first_weight, flipped(second_weight))
    act = jax.nn.silu(pre).astype(jnp.bfloat16)
    sigma = jax.nn.sigmoid(pre)
    act_grad = (back * (sigma * (1.0 + pre * (1.0 - sigma)))).astype(jnp.bfloat16)
    both = jnp.concatenate([act, act_grad], axis=-1)
    features, input_grad = convolve_pair(both, owned, second_weight, flipped(first_weight))
    features = jnp.transpose(features.astype(jnp.bfloat16), (3, 0, 1, 2))
    input_grad = jnp.transpose(input_grad.astype(jnp.bfloat16), (3, 0, 1, 2))
    return (features, input_grad)


def solution(mesh):
    placed = (P("col", None, "gx", "gy"), P("col", None, "gx", "gy"), P(), P())
    return jax.shard_map(
        on_device,
        mesh=mesh,
        in_specs=placed,
        out_specs=(P("col", None, "gx", "gy"), P("col", None, "gx", "gy")),
        check_vma=False,
    )
```

```python
import jax
import jax.numpy as jnp
from jax import lax
from jax.sharding import PartitionSpec as P


def ring(axis, step):
    n = lax.axis_size(axis)
    return [(i, (i + step) % n) for i in range(n)]


def halos(block):
    C, Z, X, Y = block.shape
    lo_x = lax.ppermute(block[:, :, X - 1, :].reshape(C * Z, Y), "gx", ring("gx", 1))
    hi_x = lax.ppermute(block[:, :, 0, :].reshape(C * Z, Y), "gx", ring("gx", -1))
    ext = jnp.concatenate([lo_x.reshape(C, Z, 1, Y), block, hi_x.reshape(C, Z, 1, Y)], axis=2)
    rows = C * Z * (X + 2)
    lo_y = lax.ppermute(ext[:, :, :, Y - 1].reshape(-1, 128), "gy", ring("gy", 1))
    hi_y = lax.ppermute(ext[:, :, :, 0].reshape(-1, 128), "gy", ring("gy", -1))
    return lo_x, hi_x, lo_y, hi_y


def assemble(block, lo_x, hi_x, lo_y, hi_y):
    C, Z, X, Y = block.shape
    ext = jnp.concatenate([lo_x.reshape(C, Z, 1, Y), block, hi_x.reshape(C, Z, 1, Y)], axis=2)
    left = lo_y.reshape(C, Z, X + 2, 1)
    right = hi_y.reshape(C, Z, X + 2, 1)
    return jnp.concatenate([left, ext, right], axis=3)


def padded_pair(block):
    C, Z, X, Y = block.shape
    swap = [(0, 1), (1, 0)]
    other = lax.ppermute(block.reshape(C * Z * X, Y), "col", swap).reshape(block.shape)
    pieces = halos(block)
    message = jnp.concatenate(pieces, axis=0)
    got = lax.ppermute(message, "col", swap)
    theirs = []
    at = 0
    for p in pieces:
        theirs.append(got[at:at + p.shape[0]])
        at += p.shape[0]
    return assemble(block, *pieces), assemble(other, *theirs)


def local_conv(piece, weight):
    result = lax.conv_general_dilated(
        jnp.transpose(piece, (1, 2, 3, 0))[None],
        weight,
        (1, 1, 1),
        ((1, 1), (0, 0), (0, 0)),
        dimension_numbers=("NDHWC", "DHWIO", "NDHWC"),
        preferred_element_type=jnp.float32,
    )
    return result[0]


def flipped(weight):
    return jnp.transpose(jnp.flip(weight, (2, 3, 4)), (1, 0, 2, 3, 4))


def ordered(weight, owned):
    col = lax.axis_index("col")
    rows = lax.dynamic_slice_in_dim(weight, col * owned, owned, 0)
    mine = lax.dynamic_slice_in_dim(rows, col * owned, owned, 1)
    other = lax.dynamic_slice_in_dim(rows, (1 - col) * owned, owned, 1)
    return jnp.transpose(jnp.concatenate([mine, other], axis=1), (2, 3, 4, 1, 0))


def convolve_pair(a, b, wa, wb):
    owned = a.shape[0]
    padded, partner = padded_pair(jnp.concatenate([a, b], axis=0))
    fa = jnp.concatenate([padded[:owned], partner[:owned]], axis=0)
    fb = jnp.concatenate([padded[owned:], partner[owned:]], axis=0)
    return local_conv(fa, ordered(wa, owned)), local_conv(fb, ordered(wb, owned))


def on_device(inputs, cotangent, first_weight, second_weight):
    pre, back = convolve_pair(inputs, cotangent, first_weight, flipped(second_weight))
    act = jax.nn.silu(pre).astype(jnp.bfloat16)
    sigma = jax.nn.sigmoid(pre)
    act_grad = (back * (sigma * (1.0 + pre * (1.0 - sigma)))).astype(jnp.bfloat16)
    to_ncdhw = lambda v: jnp.transpose(v, (3, 0, 1, 2))
    features, input_grad = convolve_pair(to_ncdhw(act), to_ncdhw(act_grad), second_weight, flipped(first_weight))
    return (to_ncdhw(features.astype(jnp.bfloat16)), to_ncdhw(input_grad.astype(jnp.bfloat16)))


def solution(mesh):
    placed = (P("col", None, "gx", "gy"), P("col", None, "gx", "gy"), P(), P())
    return jax.shard_map(
        on_device,
        mesh=mesh,
        in_specs=placed,
        out_specs=(P("col", None, "gx", "gy"), P("col", None, "gx", "gy")),
        check_vma=False,
    )
```

```python
import jax
import jax.numpy as jnp
from jax import lax
from jax.sharding import PartitionSpec as P


def ring(axis, step):
    n = lax.axis_size(axis)
    return [(i, (i + step) % n) for i in range(n)]


def halos(block):
    C, Z, X, Y = block.shape
    lo_x = lax.ppermute(block[:, :, X - 1, :].reshape(C * Z, Y), "gx", ring("gx", 1))
    hi_x = lax.ppermute(block[:, :, 0, :].reshape(C * Z, Y), "gx", ring("gx", -1))
    ext = jnp.concatenate([lo_x.reshape(C, Z, 1, Y), block, hi_x.reshape(C, Z, 1, Y)], axis=2)
    rows = C * Z * (X + 2)
    lo_y = lax.ppermute(ext[:, :, :, Y - 1].reshape(-1, 128), "gy", ring("gy", 1))
    hi_y = lax.ppermute(ext[:, :, :, 0].reshape(-1, 128), "gy", ring("gy", -1))
    return lo_x, hi_x, lo_y, hi_y


def assemble(block, lo_x, hi_x, lo_y, hi_y):
    C, Z, X, Y = block.shape
    ext = jnp.concatenate([lo_x.reshape(C, Z, 1, Y), block, hi_x.reshape(C, Z, 1, Y)], axis=2)
    left = lo_y.reshape(C, Z, X + 2, 1)
    right = hi_y.reshape(C, Z, X + 2, 1)
    return jnp.concatenate([left, ext, right], axis=3)


def padded_pair(block):
    C, Z, X, Y = block.shape
    swap = [(0, 1), (1, 0)]
    other = lax.ppermute(block.reshape(C * Z * X, Y), "col", swap).reshape(block.shape)
    pieces = halos(block)
    message = jnp.concatenate(pieces, axis=0)
    got = lax.ppermute(message, "col", swap)
    theirs = []
    at = 0
    for p in pieces:
        theirs.append(got[at:at + p.shape[0]])
        at += p.shape[0]
    return assemble(block, *pieces), assemble(other, *theirs)


def local_conv(piece, weight):
    I, Z, X2, Y2 = piece.shape
    D, H, W, _, O = weight.shape
    Y = Y2 - W + 1
    t = jnp.transpose(piece, (1, 2, 3, 0))
    shifted = jnp.concatenate([t[:, :, c:c + Y, :] for c in range(W)], axis=-1)
    result = lax.conv_general_dilated(
        shifted[None],
        weight.reshape(D, H, 1, W * I, O),
        (1, 1, 1),
        ((1, 1), (0, 0), (0, 0)),
        dimension_numbers=("NDHWC", "DHWIO", "NDHWC"),
        preferred_element_type=jnp.float32,
    )
    return result[0]


def flipped(weight):
    return jnp.transpose(jnp.flip(weight, (2, 3, 4)), (1, 0, 2, 3, 4))


def ordered(weight, owned):
    col = lax.axis_index("col")
    rows = lax.dynamic_slice_in_dim(weight, col * owned, owned, 0)
    mine = lax.dynamic_slice_in_dim(rows, col * owned, owned, 1)
    other = lax.dynamic_slice_in_dim(rows, (1 - col) * owned, owned, 1)
    return jnp.transpose(jnp.concatenate([mine, other], axis=1), (2, 3, 4, 1, 0))


def convolve_pair(a, b, wa, wb):
    owned = a.shape[0]
    padded, partner = padded_pair(jnp.concatenate([a, b], axis=0))
    fa = jnp.concatenate([padded[:owned], partner[:owned]], axis=0)
    fb = jnp.concatenate([padded[owned:], partner[owned:]], axis=0)
    return local_conv(fa, ordered(wa, owned)), local_conv(fb, ordered(wb, owned))


def on_device(inputs, cotangent, first_weight, second_weight):
    pre, back = convolve_pair(inputs, cotangent, first_weight, flipped(second_weight))
    act = jax.nn.silu(pre).astype(jnp.bfloat16)
    sigma = jax.nn.sigmoid(pre)
    act_grad = (back * (sigma * (1.0 + pre * (1.0 - sigma)))).astype(jnp.bfloat16)
    to_ncdhw = lambda v: jnp.transpose(v, (3, 0, 1, 2))
    features, input_grad = convolve_pair(to_ncdhw(act), to_ncdhw(act_grad), second_weight, flipped(first_weight))
    return (to_ncdhw(features.astype(jnp.bfloat16)), to_ncdhw(input_grad.astype(jnp.bfloat16)))


def solution(mesh):
    placed = (P("col", None, "gx", "gy"), P("col", None, "gx", "gy"), P(), P())
    return jax.shard_map(
        on_device,
        mesh=mesh,
        in_specs=placed,
        out_specs=(P("col", None, "gx", "gy"), P("col", None, "gx", "gy")),
        check_vma=False,
    )
```

```python
import jax
import jax.numpy as jnp
from jax import lax
from jax.sharding import PartitionSpec as P


def ring(axis, step):
    n = lax.axis_size(axis)
    return [(i, (i + step) % n) for i in range(n)]


def flat128(v):
    v = v.reshape(-1)
    return jnp.pad(v, (0, (-v.shape[0]) % 128)).reshape(-1, 128)


def halos(block, w):
    C, Z, X, Y = block.shape
    lo_x = lax.ppermute(block[:, :, X - w:, :].reshape(C * Z * w, Y), "gx", ring("gx", 1))
    hi_x = lax.ppermute(block[:, :, :w, :].reshape(C * Z * w, Y), "gx", ring("gx", -1))
    ext = jnp.concatenate([lo_x.reshape(C, Z, w, Y), block, hi_x.reshape(C, Z, w, Y)], axis=2)
    lo_y = lax.ppermute(flat128(ext[:, :, :, Y - w:]), "gy", ring("gy", 1))
    hi_y = lax.ppermute(flat128(ext[:, :, :, :w]), "gy", ring("gy", -1))
    return lo_x, hi_x, lo_y, hi_y


def assemble(block, w, lo_x, hi_x, lo_y, hi_y):
    C, Z, X, Y = block.shape
    ext = jnp.concatenate([lo_x.reshape(C, Z, w, Y), block, hi_x.reshape(C, Z, w, Y)], axis=2)
    n = C * Z * (X + 2 * w) * w
    left = lo_y.reshape(-1)[:n].reshape(C, Z, X + 2 * w, w)
    right = hi_y.reshape(-1)[:n].reshape(C, Z, X + 2 * w, w)
    return jnp.concatenate([left, ext, right], axis=3)


SWAP = [(0, 1), (1, 0)]


def padded_pair(block, w):
    C, Z, X, Y = block.shape
    other = lax.ppermute(block.reshape(C * Z * X, Y), "col", SWAP).reshape(block.shape)
    pieces = halos(block, w)
    message = jnp.concatenate(pieces, axis=0)
    got = lax.ppermute(message, "col", SWAP)
    theirs = []
    at = 0
    for p in pieces:
        theirs.append(got[at:at + p.shape[0]])
        at += p.shape[0]
    return assemble(block, w, *pieces), assemble(other, w, *theirs)


def local_conv(t, weight):
    Z, X2, Y2, I = t.shape
    D, H, W, _, O = weight.shape
    Y = Y2 - W + 1
    shifted = jnp.concatenate([t[:, :, c:c + Y, :] for c in range(W)], axis=-1)
    result = lax.conv_general_dilated(
        shifted[None],
        weight.reshape(D, H, 1, W * I, O),
        (1, 1, 1),
        ((1, 1), (0, 0), (0, 0)),
        dimension_numbers=("NDHWC", "DHWIO", "NDHWC"),
        preferred_element_type=jnp.float32,
    )
    return result[0]


def flipped(weight):
    return jnp.transpose(jnp.flip(weight, (2, 3, 4)), (1, 0, 2, 3, 4))


def ordered(weight, owned):
    col = lax.axis_index("col")
    rows = lax.dynamic_slice_in_dim(weight, col * owned, owned, 0)
    mine = lax.dynamic_slice_in_dim(rows, col * owned, owned, 1)
    other = lax.dynamic_slice_in_dim(rows, (1 - col) * owned, owned, 1)
    return jnp.transpose(jnp.concatenate([mine, other], axis=1), (2, 3, 4, 1, 0))


def first_pair(a, b, wa, wb):
    owned = a.shape[0]
    padded, partner = padded_pair(jnp.concatenate([a, b], axis=0), 2)
    to_ndhwc = lambda v: jnp.transpose(v, (1, 2, 3, 0))
    fa = to_ndhwc(jnp.concatenate([padded[:owned], partner[:owned]], axis=0))
    fb = to_ndhwc(jnp.concatenate([padded[owned:], partner[owned:]], axis=0))
    return local_conv(fa, ordered(wa, owned)), local_conv(fb, ordered(wb, owned))


def second_pair(a, b, wa, wb):
    owned = a.shape[-1]
    both = jnp.concatenate([a, b], axis=-1)
    other = lax.ppermute(flat128(both), "col", SWAP).reshape(-1)[: both.size].reshape(both.shape)
    fa = jnp.concatenate([both[..., :owned], other[..., :owned]], axis=-1)
    fb = jnp.concatenate([both[..., owned:], other[..., owned:]], axis=-1)
    return local_conv(fa, ordered(wa, owned)), local_conv(fb, ordered(wb, owned))


def on_device(inputs, cotangent, first_weight, second_weight):
    pre, back = first_pair(inputs, cotangent, first_weight, flipped(second_weight))
    act = jax.nn.silu(pre).astype(jnp.bfloat16)
    sigma = jax.nn.sigmoid(pre)
    act_grad = (back * (sigma * (1.0 + pre * (1.0 - sigma)))).astype(jnp.bfloat16)
    features, input_grad = second_pair(act, act_grad, second_weight, flipped(first_weight))
    to_ncdhw = lambda v: jnp.transpose(v, (3, 0, 1, 2))
    return (to_ncdhw(features.astype(jnp.bfloat16)), to_ncdhw(input_grad.astype(jnp.bfloat16)))


def solution(mesh):
    placed = (P("col", None, "gx", "gy"), P("col", None, "gx", "gy"), P(), P())
    return jax.shard_map(
        on_device,
        mesh=mesh,
        in_specs=placed,
        out_specs=(P("col", None, "gx", "gy"), P("col", None, "gx", "gy")),
        check_vma=False,
    )
```

```python
import jax
import jax.numpy as jnp
from jax import lax
from jax.sharding import PartitionSpec as P


def ring(axis, step):
    n = lax.axis_size(axis)
    return [(i, (i + step) % n) for i in range(n)]


def halos(block):
    C, Z, X, Y = block.shape
    lo_x = lax.ppermute(block[:, :, X - 1, :].reshape(C * Z, Y), "gx", ring("gx", 1))
    hi_x = lax.ppermute(block[:, :, 0, :].reshape(C * Z, Y), "gx", ring("gx", -1))
    ext = jnp.concatenate([lo_x.reshape(C, Z, 1, Y), block, hi_x.reshape(C, Z, 1, Y)], axis=2)
    rows = C * Z * (X + 2)
    lo_y = lax.ppermute(ext[:, :, :, Y - 1].reshape(-1, 128), "gy", ring("gy", 1))
    hi_y = lax.ppermute(ext[:, :, :, 0].reshape(-1, 128), "gy", ring("gy", -1))
    return lo_x, hi_x, lo_y, hi_y


def assemble(block, lo_x, hi_x, lo_y, hi_y):
    C, Z, X, Y = block.shape
    ext = jnp.concatenate([lo_x.reshape(C, Z, 1, Y), block, hi_x.reshape(C, Z, 1, Y)], axis=2)
    left = lo_y.reshape(C, Z, X + 2, 1)
    right = hi_y.reshape(C, Z, X + 2, 1)
    return jnp.concatenate([left, ext, right], axis=3)


def padded_full(block):
    C, Z, X, Y = block.shape
    other = lax.ppermute(block.reshape(C * Z * X, Y), "col", [(0, 1), (1, 0)]).reshape(block.shape)
    full = jnp.concatenate([block, other], axis=0)
    return assemble(full, *halos(full))


def local_conv(piece, weight):
    I, Z, X2, Y2 = piece.shape
    D, H, W, _, O = weight.shape
    Y = Y2 - W + 1
    t = jnp.transpose(piece, (1, 2, 3, 0))
    shifted = jnp.concatenate([t[:, :, c:c + Y, :] for c in range(W)], axis=-1)
    result = lax.conv_general_dilated(
        shifted[None],
        weight.reshape(D, H, 1, W * I, O),
        (1, 1, 1),
        ((1, 1), (0, 0), (0, 0)),
        dimension_numbers=("NDHWC", "DHWIO", "NDHWC"),
        preferred_element_type=jnp.float32,
    )
    return result[0]


def flipped(weight):
    return jnp.transpose(jnp.flip(weight, (2, 3, 4)), (1, 0, 2, 3, 4))


def ordered(weight, owned):
    col = lax.axis_index("col")
    rows = lax.dynamic_slice_in_dim(weight, col * owned, owned, 0)
    mine = lax.dynamic_slice_in_dim(rows, col * owned, owned, 1)
    other = lax.dynamic_slice_in_dim(rows, (1 - col) * owned, owned, 1)
    return jnp.transpose(jnp.concatenate([mine, other], axis=1), (2, 3, 4, 1, 0))


def convolve_pair(a, b, wa, wb):
    owned = a.shape[0]
    padded = padded_full(jnp.concatenate([a, b], axis=0))
    fa = jnp.concatenate([padded[:owned], padded[2 * owned:3 * owned]], axis=0)
    fb = jnp.concatenate([padded[owned:2 * owned], padded[3 * owned:]], axis=0)
    return local_conv(fa, ordered(wa, owned)), local_conv(fb, ordered(wb, owned))


def on_device(inputs, cotangent, first_weight, second_weight):
    pre, back = convolve_pair(inputs, cotangent, first_weight, flipped(second_weight))
    act = jax.nn.silu(pre).astype(jnp.bfloat16)
    sigma = jax.nn.sigmoid(pre)
    act_grad = (back * (sigma * (1.0 + pre * (1.0 - sigma)))).astype(jnp.bfloat16)
    to_ncdhw = lambda v: jnp.transpose(v, (3, 0, 1, 2))
    features, input_grad = convolve_pair(to_ncdhw(act), to_ncdhw(act_grad), second_weight, flipped(first_weight))
    return (to_ncdhw(features.astype(jnp.bfloat16)), to_ncdhw(input_grad.astype(jnp.bfloat16)))


def solution(mesh):
    placed = (P("col", None, "gx", "gy"), P("col", None, "gx", "gy"), P(), P())
    return jax.shard_map(
        on_device,
        mesh=mesh,
        in_specs=placed,
        out_specs=(P("col", None, "gx", "gy"), P("col", None, "gx", "gy")),
        check_vma=False,
    )
```

```python
import jax
import jax.numpy as jnp
from jax import lax
from jax.sharding import PartitionSpec as P


def ring(axis, step):
    n = lax.axis_size(axis)
    return [(i, (i + step) % n) for i in range(n)]


SWAP = [(0, 1), (1, 0)]


def halos(t):
    Z, X, Y, C = t.shape
    lo_x = lax.ppermute(t[:, X - 1], "gx", ring("gx", 1))
    hi_x = lax.ppermute(t[:, 0], "gx", ring("gx", -1))
    ext = jnp.concatenate([lo_x[:, None], t, hi_x[:, None]], axis=1)
    lo_y = lax.ppermute(ext[:, :, Y - 1], "gy", ring("gy", 1))
    hi_y = lax.ppermute(ext[:, :, 0], "gy", ring("gy", -1))
    return lo_x, hi_x, lo_y, hi_y


def assemble(t, lo_x, hi_x, lo_y, hi_y):
    ext = jnp.concatenate([lo_x[:, None], t, hi_x[:, None]], axis=1)
    return jnp.concatenate([lo_y[:, :, None], ext, hi_y[:, :, None]], axis=2)


def padded_pair(block, t):
    C, Z, X, Y = block.shape
    got = lax.ppermute(block.reshape(C * Z * X, Y), "col", SWAP).reshape(block.shape)
    other = jnp.transpose(got, (1, 2, 3, 0))
    pieces = halos(t)
    message = jnp.concatenate([p.reshape(-1, C) for p in pieces], axis=0)
    got = lax.ppermute(message, "col", SWAP)
    theirs = []
    at = 0
    for p in pieces:
        n = p.size // C
        theirs.append(got[at:at + n].reshape(p.shape))
        at += n
    return assemble(t, *pieces), assemble(other, *theirs)


def local_conv(t, weight):
    Z, X2, Y2, I = t.shape
    D, H, W, _, O = weight.shape
    Y = Y2 - W + 1
    shifted = jnp.concatenate([t[:, :, c:c + Y, :] for c in range(W)], axis=-1)
    result = lax.conv_general_dilated(
        shifted[None],
        weight.reshape(D, H, 1, W * I, O),
        (1, 1, 1),
        ((1, 1), (0, 0), (0, 0)),
        dimension_numbers=("NDHWC", "DHWIO", "NDHWC"),
        preferred_element_type=jnp.float32,
    )
    return result[0]


def flipped(weight):
    return jnp.transpose(jnp.flip(weight, (2, 3, 4)), (1, 0, 2, 3, 4))


def ordered(weight, owned):
    col = lax.axis_index("col")
    rows = lax.dynamic_slice_in_dim(weight, col * owned, owned, 0)
    mine = lax.dynamic_slice_in_dim(rows, col * owned, owned, 1)
    other = lax.dynamic_slice_in_dim(rows, (1 - col) * owned, owned, 1)
    return jnp.transpose(jnp.concatenate([mine, other], axis=1), (2, 3, 4, 1, 0))


def convolve_pair(block, t, owned, wa, wb):
    padded, partner = padded_pair(block, t)
    fa = jnp.concatenate([padded[..., :owned], partner[..., :owned]], axis=-1)
    fb = jnp.concatenate([padded[..., owned:], partner[..., owned:]], axis=-1)
    return local_conv(fa, ordered(wa, owned)), local_conv(fb, ordered(wb, owned))


def on_device(inputs, cotangent, first_weight, second_weight):
    owned = inputs.shape[0]
    to_ndhwc = lambda v: jnp.transpose(v, (1, 2, 3, 0))
    to_ncdhw = lambda v: jnp.transpose(v, (3, 0, 1, 2))
    block = jnp.concatenate([inputs, cotangent], axis=0)
    pre, back = convolve_pair(block, to_ndhwc(block), owned, first_weight, flipped(second_weight))
    act = jax.nn.silu(pre).astype(jnp.bfloat16)
    sigma = jax.nn.sigmoid(pre)
    act_grad = (back * (sigma * (1.0 + pre * (1.0 - sigma)))).astype(jnp.bfloat16)
    t = jnp.concatenate([act, act_grad], axis=-1)
    features, input_grad = convolve_pair(to_ncdhw(t), t, owned, second_weight, flipped(first_weight))
    return (to_ncdhw(features.astype(jnp.bfloat16)), to_ncdhw(input_grad.astype(jnp.bfloat16)))


def solution(mesh):
    placed = (P("col", None, "gx", "gy"), P("col", None, "gx", "gy"), P(), P())
    return jax.shard_map(
        on_device,
        mesh=mesh,
        in_specs=placed,
        out_specs=(P("col", None, "gx", "gy"), P("col", None, "gx", "gy")),
        check_vma=False,
    )
```

```python
import jax
import jax.numpy as jnp
from jax import lax
from jax.sharding import PartitionSpec as P


def ring(axis, step):
    n = lax.axis_size(axis)
    return [(i, (i + step) % n) for i in range(n)]


def halos(block):
    C, Z, X, Y = block.shape
    lo_x = lax.ppermute(block[:, :, X - 1, :].reshape(C * Z, Y), "gx", ring("gx", 1))
    hi_x = lax.ppermute(block[:, :, 0, :].reshape(C * Z, Y), "gx", ring("gx", -1))
    ext = jnp.concatenate([lo_x.reshape(C, Z, 1, Y), block, hi_x.reshape(C, Z, 1, Y)], axis=2)
    rows = C * Z * (X + 2)
    lo_y = lax.ppermute(ext[:, :, :, Y - 1].reshape(-1, 128), "gy", ring("gy", 1))
    hi_y = lax.ppermute(ext[:, :, :, 0].reshape(-1, 128), "gy", ring("gy", -1))
    return lo_x, hi_x, lo_y, hi_y


def assemble(block, lo_x, hi_x, lo_y, hi_y):
    C, Z, X, Y = block.shape
    ext = jnp.concatenate([lo_x.reshape(C, Z, 1, Y), block, hi_x.reshape(C, Z, 1, Y)], axis=2)
    left = lo_y.reshape(C, Z, X + 2, 1)
    right = hi_y.reshape(C, Z, X + 2, 1)
    return jnp.concatenate([left, ext, right], axis=3)


def padded_pair(block):
    C, Z, X, Y = block.shape
    swap = [(0, 1), (1, 0)]
    other = lax.ppermute(block.reshape(C * Z * X, Y), "col", swap).reshape(block.shape)
    pieces = halos(block)
    message = jnp.concatenate(pieces, axis=0)
    got = lax.ppermute(message, "col", swap)
    theirs = []
    at = 0
    for p in pieces:
        theirs.append(got[at:at + p.shape[0]])
        at += p.shape[0]
    return assemble(block, *pieces), assemble(other, *theirs)


def local_conv(piece, weight):
    I, Z, X2, Y2 = piece.shape
    D, H, W, _, O = weight.shape
    Y = Y2 - W + 1
    t = jnp.transpose(piece, (1, 2, 3, 0))
    shifted = jnp.concatenate([t[:, :, c:c + Y, :] for c in range(W)], axis=-1)
    result = lax.conv_general_dilated(
        shifted[None],
        weight.reshape(D, H, 1, W * I, O),
        (1, 1, 1),
        ((1, 1), (0, 0), (0, 0)),
        dimension_numbers=("NDHWC", "DHWIO", "NCDHW"),
        preferred_element_type=jnp.float32,
    )
    return result[0]


def flipped(weight):
    return jnp.transpose(jnp.flip(weight, (2, 3, 4)), (1, 0, 2, 3, 4))


def ordered(weight, owned):
    col = lax.axis_index("col")
    rows = lax.dynamic_slice_in_dim(weight, col * owned, owned, 0)
    mine = lax.dynamic_slice_in_dim(rows, col * owned, owned, 1)
    other = lax.dynamic_slice_in_dim(rows, (1 - col) * owned, owned, 1)
    return jnp.transpose(jnp.concatenate([mine, other], axis=1), (2, 3, 4, 1, 0))


def convolve_pair(a, b, wa, wb):
    owned = a.shape[0]
    padded, partner = padded_pair(jnp.concatenate([a, b], axis=0))
    fa = jnp.concatenate([padded[:owned], partner[:owned]], axis=0)
    fb = jnp.concatenate([padded[owned:], partner[owned:]], axis=0)
    return local_conv(fa, ordered(wa, owned)), local_conv(fb, ordered(wb, owned))


def on_device(inputs, cotangent, first_weight, second_weight):
    pre, back = convolve_pair(inputs, cotangent, first_weight, flipped(second_weight))
    act = jax.nn.silu(pre).astype(jnp.bfloat16)
    sigma = jax.nn.sigmoid(pre)
    act_grad = (back * (sigma * (1.0 + pre * (1.0 - sigma)))).astype(jnp.bfloat16)
    features, input_grad = convolve_pair(act, act_grad, second_weight, flipped(first_weight))
    return (features.astype(jnp.bfloat16), input_grad.astype(jnp.bfloat16))


def solution(mesh):
    placed = (P("col", None, "gx", "gy"), P("col", None, "gx", "gy"), P(), P())
    return jax.shard_map(
        on_device,
        mesh=mesh,
        in_specs=placed,
        out_specs=(P("col", None, "gx", "gy"), P("col", None, "gx", "gy")),
        check_vma=False,
    )
```

```python
import jax
import jax.numpy as jnp
from jax import lax
from jax.sharding import PartitionSpec as P


def ring(axis, step):
    n = lax.axis_size(axis)
    return [(i, (i + step) % n) for i in range(n)]


def halos(parts):
    block = jnp.concatenate(parts, axis=0)
    C, Z, X, Y = block.shape
    row = lambda i: jnp.concatenate([p[:, :, i, :] for p in parts], axis=0).reshape(C * Z, Y)
    lo_x = lax.ppermute(row(X - 1), "gx", ring("gx", 1))
    hi_x = lax.ppermute(row(0), "gx", ring("gx", -1))
    ext = jnp.concatenate([lo_x.reshape(C, Z, 1, Y), block, hi_x.reshape(C, Z, 1, Y)], axis=2)
    lo_y = lax.ppermute(ext[:, :, :, Y - 1].reshape(-1, 128), "gy", ring("gy", 1))
    hi_y = lax.ppermute(ext[:, :, :, 0].reshape(-1, 128), "gy", ring("gy", -1))
    return lo_x, hi_x, lo_y, hi_y


def assemble(block, lo_x, hi_x, lo_y, hi_y):
    C, Z, X, Y = block.shape
    ext = jnp.concatenate([lo_x.reshape(C, Z, 1, Y), block, hi_x.reshape(C, Z, 1, Y)], axis=2)
    left = lo_y.reshape(C, Z, X + 2, 1)
    right = hi_y.reshape(C, Z, X + 2, 1)
    return jnp.concatenate([left, ext, right], axis=3)


def padded_pair(parts):
    block = jnp.concatenate(parts, axis=0)
    C, Z, X, Y = block.shape
    swap = [(0, 1), (1, 0)]
    other = lax.ppermute(block.reshape(C * Z * X, Y), "col", swap).reshape(block.shape)
    pieces = halos(parts)
    message = jnp.concatenate(pieces, axis=0)
    got = lax.ppermute(message, "col", swap)
    theirs = []
    at = 0
    for p in pieces:
        theirs.append(got[at:at + p.shape[0]])
        at += p.shape[0]
    return assemble(block, *pieces), assemble(other, *theirs)


def local_conv(piece, weight):
    I, Z, X2, Y2 = piece.shape
    D, H, W, _, O = weight.shape
    Y = Y2 - W + 1
    t = jnp.transpose(piece, (1, 2, 3, 0))
    shifted = jnp.concatenate([t[:, :, c:c + Y, :] for c in range(W)], axis=-1)
    result = lax.conv_general_dilated(
        shifted[None],
        weight.reshape(D, H, 1, W * I, O),
        (1, 1, 1),
        ((1, 1), (0, 0), (0, 0)),
        dimension_numbers=("NDHWC", "DHWIO", "NDHWC"),
        preferred_element_type=jnp.float32,
    )
    return result[0]


def flipped(weight):
    return jnp.transpose(jnp.flip(weight, (2, 3, 4)), (1, 0, 2, 3, 4))


def ordered(weight, owned):
    col = lax.axis_index("col")
    rows = lax.dynamic_slice_in_dim(weight, col * owned, owned, 0)
    mine = lax.dynamic_slice_in_dim(rows, col * owned, owned, 1)
    other = lax.dynamic_slice_in_dim(rows, (1 - col) * owned, owned, 1)
    return jnp.transpose(jnp.concatenate([mine, other], axis=1), (2, 3, 4, 1, 0))


def convolve_pair(a, b, wa, wb):
    owned = a.shape[0]
    padded, partner = padded_pair((a, b))
    fa = jnp.concatenate([padded[:owned], partner[:owned]], axis=0)
    fb = jnp.concatenate([padded[owned:], partner[owned:]], axis=0)
    return local_conv(fa, ordered(wa, owned)), local_conv(fb, ordered(wb, owned))


def on_device(inputs, cotangent, first_weight, second_weight):
    pre, back = convolve_pair(inputs, cotangent, first_weight, flipped(second_weight))
    act = jax.nn.silu(pre).astype(jnp.bfloat16)
    sigma = jax.nn.sigmoid(pre)
    act_grad = (back * (sigma * (1.0 + pre * (1.0 - sigma)))).astype(jnp.bfloat16)
    to_ncdhw = lambda v: jnp.transpose(v, (3, 0, 1, 2))
    features, input_grad = convolve_pair(to_ncdhw(act), to_ncdhw(act_grad), second_weight, flipped(first_weight))
    return (to_ncdhw(features.astype(jnp.bfloat16)), to_ncdhw(input_grad.astype(jnp.bfloat16)))


def solution(mesh):
    placed = (P("col", None, "gx", "gy"), P("col", None, "gx", "gy"), P(), P())
    return jax.shard_map(
        on_device,
        mesh=mesh,
        in_specs=placed,
        out_specs=(P("col", None, "gx", "gy"), P("col", None, "gx", "gy")),
        check_vma=False,
    )
```

```python
import jax
import jax.numpy as jnp
from jax import lax
from jax.sharding import PartitionSpec as P


def ring(axis, step):
    n = lax.axis_size(axis)
    return [(i, (i + step) % n) for i in range(n)]


def cross(axis, step):
    n = lax.axis_size(axis)
    return [(i * 2 + c, ((i + step) % n) * 2 + 1 - c) for i in range(n) for c in range(2)]


def halos(block):
    C, Z, X, Y = block.shape
    lo_row = block[:, :, X - 1, :].reshape(C * Z, Y)
    hi_row = block[:, :, 0, :].reshape(C * Z, Y)
    lo_x = lax.ppermute(lo_row, "gx", ring("gx", 1))
    hi_x = lax.ppermute(hi_row, "gx", ring("gx", -1))
    lo_xc = lax.ppermute(lo_row, ("gx", "col"), cross("gx", 1))
    hi_xc = lax.ppermute(hi_row, ("gx", "col"), cross("gx", -1))
    ext = jnp.concatenate([lo_x.reshape(C, Z, 1, Y), block, hi_x.reshape(C, Z, 1, Y)], axis=2)
    lo_col = ext[:, :, :, Y - 1].reshape(-1, 128)
    hi_col = ext[:, :, :, 0].reshape(-1, 128)
    lo_y = lax.ppermute(lo_col, "gy", ring("gy", 1))
    hi_y = lax.ppermute(hi_col, "gy", ring("gy", -1))
    lo_yc = lax.ppermute(lo_col, ("gy", "col"), cross("gy", 1))
    hi_yc = lax.ppermute(hi_col, ("gy", "col"), cross("gy", -1))
    return (lo_x, hi_x, lo_y, hi_y), (lo_xc, hi_xc, lo_yc, hi_yc)


def assemble(block, lo_x, hi_x, lo_y, hi_y):
    C, Z, X, Y = block.shape
    ext = jnp.concatenate([lo_x.reshape(C, Z, 1, Y), block, hi_x.reshape(C, Z, 1, Y)], axis=2)
    left = lo_y.reshape(C, Z, X + 2, 1)
    right = hi_y.reshape(C, Z, X + 2, 1)
    return jnp.concatenate([left, ext, right], axis=3)


def padded_pair(block):
    C, Z, X, Y = block.shape
    swap = [(0, 1), (1, 0)]
    other = lax.ppermute(block.reshape(C * Z * X, Y), "col", swap).reshape(block.shape)
    pieces, theirs = halos(block)
    return assemble(block, *pieces), assemble(other, *theirs)


def local_conv(piece, weight):
    I, Z, X2, Y2 = piece.shape
    D, H, W, _, O = weight.shape
    Y = Y2 - W + 1
    t = jnp.transpose(piece, (1, 2, 3, 0))
    shifted = jnp.concatenate([t[:, :, c:c + Y, :] for c in range(W)], axis=-1)
    result = lax.conv_general_dilated(
        shifted[None],
        weight.reshape(D, H, 1, W * I, O),
        (1, 1, 1),
        ((1, 1), (0, 0), (0, 0)),
        dimension_numbers=("NDHWC", "DHWIO", "NDHWC"),
        preferred_element_type=jnp.float32,
    )
    return result[0]


def flipped(weight):
    return jnp.transpose(jnp.flip(weight, (2, 3, 4)), (1, 0, 2, 3, 4))


def ordered(weight, owned):
    col = lax.axis_index("col")
    rows = lax.dynamic_slice_in_dim(weight, col * owned, owned, 0)
    mine = lax.dynamic_slice_in_dim(rows, col * owned, owned, 1)
    other = lax.dynamic_slice_in_dim(rows, (1 - col) * owned, owned, 1)
    return jnp.transpose(jnp.concatenate([mine, other], axis=1), (2, 3, 4, 1, 0))


def convolve_pair(a, b, wa, wb):
    owned = a.shape[0]
    padded, partner = padded_pair(jnp.concatenate([a, b], axis=0))
    fa = jnp.concatenate([padded[:owned], partner[:owned]], axis=0)
    fb = jnp.concatenate([padded[owned:], partner[owned:]], axis=0)
    return local_conv(fa, ordered(wa, owned)), local_conv(fb, ordered(wb, owned))


def on_device(inputs, cotangent, first_weight, second_weight):
    pre, back = convolve_pair(inputs, cotangent, first_weight, flipped(second_weight))
    act = jax.nn.silu(pre).astype(jnp.bfloat16)
    sigma = jax.nn.sigmoid(pre)
    act_grad = (back * (sigma * (1.0 + pre * (1.0 - sigma)))).astype(jnp.bfloat16)
    to_ncdhw = lambda v: jnp.transpose(v, (3, 0, 1, 2))
    features, input_grad = convolve_pair(to_ncdhw(act), to_ncdhw(act_grad), second_weight, flipped(first_weight))
    return (to_ncdhw(features.astype(jnp.bfloat16)), to_ncdhw(input_grad.astype(jnp.bfloat16)))


def solution(mesh):
    placed = (P("col", None, "gx", "gy"), P("col", None, "gx", "gy"), P(), P())
    return jax.shard_map(
        on_device,
        mesh=mesh,
        in_specs=placed,
        out_specs=(P("col", None, "gx", "gy"), P("col", None, "gx", "gy")),
        check_vma=False,
    )
```

```python
import jax
import jax.numpy as jnp
from jax import lax
from jax.sharding import PartitionSpec as P


def ring(axis, step):
    n = lax.axis_size(axis)
    return [(i, (i + step) % n) for i in range(n)]


def halos(block):
    C, Z, X, Y = block.shape
    lo_x = lax.ppermute(block[:, :, X - 1, :].reshape(C * Z, Y), "gx", ring("gx", 1))
    hi_x = lax.ppermute(block[:, :, 0, :].reshape(C * Z, Y), "gx", ring("gx", -1))
    ext = jnp.concatenate([lo_x.reshape(C, Z, 1, Y), block, hi_x.reshape(C, Z, 1, Y)], axis=2)
    rows = C * Z * (X + 2)
    lo_y = lax.ppermute(ext[:, :, :, Y - 1].reshape(-1, 128), "gy", ring("gy", 1))
    hi_y = lax.ppermute(ext[:, :, :, 0].reshape(-1, 128), "gy", ring("gy", -1))
    return lo_x, hi_x, lo_y, hi_y


def assemble(block, lo_x, hi_x, lo_y, hi_y):
    C, Z, X, Y = block.shape
    ext = jnp.concatenate([lo_x.reshape(C, Z, 1, Y), block, hi_x.reshape(C, Z, 1, Y)], axis=2)
    left = lo_y.reshape(C, Z, X + 2, 1)
    right = hi_y.reshape(C, Z, X + 2, 1)
    return jnp.concatenate([left, ext, right], axis=3)


def local_conv(piece, weight):
    I, Z, X2, Y2 = piece.shape
    D, H, W, _, O = weight.shape
    Y = Y2 - W + 1
    t = jnp.transpose(piece, (1, 2, 3, 0))
    shifted = jnp.concatenate([t[:, :, c:c + Y, :] for c in range(W)], axis=-1)
    result = lax.conv_general_dilated(
        shifted[None],
        weight.reshape(D, H, 1, W * I, O),
        (1, 1, 1),
        ((1, 1), (0, 0), (0, 0)),
        dimension_numbers=("NDHWC", "DHWIO", "NCDHW"),
        preferred_element_type=jnp.float32,
    )
    return result[0]


def flipped(weight):
    return jnp.transpose(jnp.flip(weight, (2, 3, 4)), (1, 0, 2, 3, 4))


def own_inputs(weight, owned):
    col = lax.axis_index("col")
    return jnp.transpose(lax.dynamic_slice_in_dim(weight, col * owned, owned, 1), (2, 3, 4, 1, 0))


def summed(partial, owned):
    col = lax.axis_index("col")
    keep = lax.dynamic_slice_in_dim(partial, col * owned, owned, 0)
    send = lax.dynamic_slice_in_dim(partial, (1 - col) * owned, owned, 0)
    C, Z, X, Y = send.shape
    got = lax.ppermute(send.reshape(C * Z * X, Y), "col", [(0, 1), (1, 0)])
    return keep + got.reshape(send.shape)


def convolve_pair(a, b, wa, wb):
    owned = a.shape[0]
    block = jnp.concatenate([a, b], axis=0)
    padded = assemble(block, *halos(block))
    pa = summed(local_conv(padded[:owned], own_inputs(wa, owned)), owned)
    pb = summed(local_conv(padded[owned:], own_inputs(wb, owned)), owned)
    return pa, pb


def on_device(inputs, cotangent, first_weight, second_weight):
    pre, back = convolve_pair(inputs, cotangent, first_weight, flipped(second_weight))
    act = jax.nn.silu(pre).astype(jnp.bfloat16)
    sigma = jax.nn.sigmoid(pre)
    act_grad = (back * (sigma * (1.0 + pre * (1.0 - sigma)))).astype(jnp.bfloat16)
    features, input_grad = convolve_pair(act, act_grad, second_weight, flipped(first_weight))
    return (features.astype(jnp.bfloat16), input_grad.astype(jnp.bfloat16))


def solution(mesh):
    placed = (P("col", None, "gx", "gy"), P("col", None, "gx", "gy"), P(), P())
    return jax.shard_map(
        on_device,
        mesh=mesh,
        in_specs=placed,
        out_specs=(P("col", None, "gx", "gy"), P("col", None, "gx", "gy")),
        check_vma=False,
    )
```

```python
import jax
import jax.numpy as jnp
from jax import lax
from jax.sharding import PartitionSpec as P


def ring(axis, step):
    n = lax.axis_size(axis)
    return [(i, (i + step) % n) for i in range(n)]


def halos(block):
    C, Z, X, Y = block.shape
    lo_x = lax.ppermute(block[:, :, X - 1, :].reshape(C * Z, Y), "gx", ring("gx", 1))
    hi_x = lax.ppermute(block[:, :, 0, :].reshape(C * Z, Y), "gx", ring("gx", -1))
    ext = jnp.concatenate([lo_x.reshape(C, Z, 1, Y), block, hi_x.reshape(C, Z, 1, Y)], axis=2)
    n = Z * (X + 2)
    column = lambda j: jnp.pad(ext[:, :, :, j].reshape(C, n), ((0, 0), (0, Y - n)))
    lo_y = lax.ppermute(column(Y - 1), "gy", ring("gy", 1))
    hi_y = lax.ppermute(column(0), "gy", ring("gy", -1))
    return lo_x, hi_x, lo_y, hi_y


def assemble(block, lo_x, hi_x, lo_y, hi_y):
    C, Z, X, Y = block.shape
    ext = jnp.concatenate([lo_x.reshape(C, Z, 1, Y), block, hi_x.reshape(C, Z, 1, Y)], axis=2)
    n = Z * (X + 2)
    left = lo_y[:, :n].reshape(C, Z, X + 2, 1)
    right = hi_y[:, :n].reshape(C, Z, X + 2, 1)
    return jnp.concatenate([left, ext, right], axis=3)


def padded_pair(block):
    C, Z, X, Y = block.shape
    swap = [(0, 1), (1, 0)]
    other = lax.ppermute(block.reshape(C * Z * X, Y), "col", swap).reshape(block.shape)
    pieces = halos(block)
    message = jnp.concatenate(pieces, axis=0)
    got = lax.ppermute(message, "col", swap)
    theirs = []
    at = 0
    for p in pieces:
        theirs.append(got[at:at + p.shape[0]])
        at += p.shape[0]
    return assemble(block, *pieces), assemble(other, *theirs)


def local_conv(piece, weight):
    I, Z, X2, Y2 = piece.shape
    D, H, W, _, O = weight.shape
    Y = Y2 - W + 1
    t = jnp.transpose(piece, (1, 2, 3, 0))
    shifted = jnp.concatenate([t[:, :, c:c + Y, :] for c in range(W)], axis=-1)
    result = lax.conv_general_dilated(
        shifted[None],
        weight.reshape(D, H, 1, W * I, O),
        (1, 1, 1),
        ((1, 1), (0, 0), (0, 0)),
        dimension_numbers=("NDHWC", "DHWIO", "NDHWC"),
        preferred_element_type=jnp.float32,
    )
    return result[0]


def flipped(weight):
    return jnp.transpose(jnp.flip(weight, (2, 3, 4)), (1, 0, 2, 3, 4))


def ordered(weight, owned):
    col = lax.axis_index("col")
    rows = lax.dynamic_slice_in_dim(weight, col * owned, owned, 0)
    mine = lax.dynamic_slice_in_dim(rows, col * owned, owned, 1)
    other = lax.dynamic_slice_in_dim(rows, (1 - col) * owned, owned, 1)
    return jnp.transpose(jnp.concatenate([mine, other], axis=1), (2, 3, 4, 1, 0))


def convolve_pair(a, b, wa, wb):
    owned = a.shape[0]
    padded, partner = padded_pair(jnp.concatenate([a, b], axis=0))
    fa = jnp.concatenate([padded[:owned], partner[:owned]], axis=0)
    fb = jnp.concatenate([padded[owned:], partner[owned:]], axis=0)
    return local_conv(fa, ordered(wa, owned)), local_conv(fb, ordered(wb, owned))


def on_device(inputs, cotangent, first_weight, second_weight):
    pre, back = convolve_pair(inputs, cotangent, first_weight, flipped(second_weight))
    act = jax.nn.silu(pre).astype(jnp.bfloat16)
    sigma = jax.nn.sigmoid(pre)
    act_grad = (back * (sigma * (1.0 + pre * (1.0 - sigma)))).astype(jnp.bfloat16)
    to_ncdhw = lambda v: jnp.transpose(v, (3, 0, 1, 2))
    features, input_grad = convolve_pair(to_ncdhw(act), to_ncdhw(act_grad), second_weight, flipped(first_weight))
    return (to_ncdhw(features.astype(jnp.bfloat16)), to_ncdhw(input_grad.astype(jnp.bfloat16)))


def solution(mesh):
    placed = (P("col", None, "gx", "gy"), P("col", None, "gx", "gy"), P(), P())
    return jax.shard_map(
        on_device,
        mesh=mesh,
        in_specs=placed,
        out_specs=(P("col", None, "gx", "gy"), P("col", None, "gx", "gy")),
        check_vma=False,
    )
```
